32 devices in a mesh: region: 8 (over z, y), route: 4 (over x, core).
Axes of the slice: x: 2, y: 2, z: 4, core: 2. Of those that a mesh axis runs over, the one named last changes fastest.
Arguments:
- fill: float32 [4, 98304], P(None, ('region', 'route')), may hold values from 0 to 1
- capacity: float32 [98304], P(('region', 'route')), may hold values from 0.2 to 1
- free_time: float32 [98304], P(('region', 'route')), may hold values from 0.5 to 3
- split_share: float32 [2, 98304], P(None, ('region', 'route')), may hold values from 0.05 to 0.45
- upstream_offset: int32 [2, 98304], P(None, ('region', 'route')), may hold values from -32 to 32
- path_flow: float32 [262144], P(('region', 'route')), may hold values from 0.01 to 0.1
- anchor: int32 [262144], P(('region', 'route')), may hold values from 0 to 12287
- depart: int32 [262144], P(('region', 'route')), may hold values from 0 to 11
- od_pair: int32 [32, 8192], P(('region', 'route')), may hold values from 0 to 2047, never falling along the last dimension, each value on 1 to 8 neighbouring positions
- swap_rate: int32 [32, 2048], P(('region', 'route')), may hold values from 1 to 8
- tile_index: int32 [2048, 4], P(('region', 'route')), may hold values from 0 to 767, as said below
- incidence: bfloat16 [2048, 4, 128, 128], P(('region', 'route')), may hold values from 0 to 1, as said below
Outputs:
- density: float32 [4, 98304], P(None, ('region', 'route'))
- path_cost: float32 [262144], P(('region', 'route'))
- new_flow: float32 [262144], P(('region', 'route'))
The draws below stay inside these ranges and needn't reach their ends.
Inputs may be any that keep to these rules, and one draw needn't show every extreme that they name: `tile_index`: each device's path tiles name, with repeats, at most 16 link tiles held by any one device, and in every draw each device names exactly 16 tiles of some device. `incidence`: the first touched tile of every path tile gives each of its paths a share of at least 0.2 on one link; all shares are 0 or at least 0.2.
All inputs are finite; a program needn't handle non-finite values.
Results may differ from the reference program's by a relative error of at most 0.00034.
Values may be sent and summed in bfloat16 or wider, within the bound.
No kernel may reach another device: no remote copies, remote signals or barrier semaphores. Data moves between devices by JAX's collectives and lax.ppermute only.
A program may use at most 128 MiB of HBM per device.

```python
import math
import jax
import jax.numpy as jnp
import numpy as np
from jax import lax

NC = 4
BND = 32
ISTEPS = 5
NI = 12
TPT = 4
OD_MOST = 8
LINK_DEV = 3072
PATH_DEV = 8192
BLOCKS = 32
LINKS = 98304
PATHS = 262144
LT_DEV = 24
PTILE_DEV = 64
PTILES = 2048
REFS = 256
CAP = 16
ODS_DEV = 2048
N_ROUTE = 4


def draw_tile_index(key, part):

    def one_block(block_key):
        first, second, third, fourth = jax.random.split(block_key, 4)
        full_owner = jax.random.randint(first, (), 0, BLOCKS)
        slots = jax.random.permutation(second, BLOCKS * CAP)
        flagged = (slots // CAP == full_owner).astype(jnp.int32)
        order = jnp.argsort(flagged, stable=True)
        others = slots[order][:REFS - CAP] // CAP
        owners = jnp.concatenate([jnp.full((CAP,), full_owner, jnp.int32), others.astype(jnp.int32)])
        owners = jax.random.permutation(fourth, owners)
        local = jax.random.randint(third, (REFS,), 0, LT_DEV)
        return (owners * LT_DEV + local).astype(jnp.int32).reshape(PTILE_DEV, TPT)
    keys = jax.random.split(jax.random.fold_in(key, 11), BLOCKS)
    return jax.vmap(one_block)(keys).reshape(PTILES, TPT)


def draw_incidence(key, part):
    first, second = jax.random.split(jax.random.fold_in(key, 23))
    shape = (PTILES, TPT, 128, 128)
    used = jax.random.uniform(first, shape) < 0.34
    value = jax.random.uniform(second, shape, jnp.float32, 0.3, 1.0)
    diagonal = jnp.arange(128)[:, None] == jnp.arange(128)[None, :]
    first_tile = (jnp.arange(TPT) == 0)[:, None, None]
    keep = used | diagonal[None, None] & first_tile[None]
    return jnp.where(keep, value, 0.0).astype(jnp.bfloat16)


def with_ends(values, rng, low, largest):
    index_at = [jax.random.randint(jax.random.fold_in(rng, axis), (), 0, length) for axis, length in enumerate(values.shape)]
    longest = values.shape.index(max(values.shape))
    neighbour = index_at[:longest] + [(index_at[longest] + 1) % values.shape[longest]] + index_at[longest + 1:]
    return values.at[tuple(index_at)].set(low).at[tuple(neighbour)].set(largest)


def block_levels(rng, shape, cuts, least, top_value):
    def one(position, parts):
        steps = jax.random.uniform(jax.random.fold_in(jax.random.fold_in(rng, 6), position), (parts,), jnp.float32, least / len(cuts), top_value / len(cuts))
        return jnp.repeat(jnp.exp(steps), shape[position] // parts).reshape((-1,) + (1,) * (len(shape) - position - 1))

    level = one(*cuts[0])
    for cut in cuts[1:]:
        level = level * one(*cut)
    return level


def length_profile(number_of, total, most, skew):
    loads = [(1 << 20) // math.isqrt(rank ** skew) + 1 for rank in range(2, number_of + 1)]
    surplus, counts = total - most - (number_of - 1), [1] * (number_of - 1)
    while surplus > 0:
        candidates = [i for i in range(number_of - 1) if counts[i] < most]
        pool, left = sum([loads[i] for i in candidates]), surplus
        for i in candidates:
            more = min(most - counts[i], max(1, left * loads[i] // pool), surplus)
            counts[i] = counts[i] + more
            surplus = surplus - more
    return np.array([most] + counts)


def ragged_sizes(stream_key, number_of, total, most, skew):
    if number_of == 2:
        one = jax.random.randint(stream_key, (), max(1, total - most), min(most, total - 1) + 1)
        return jnp.stack([one, total - one])
    tallies = jnp.asarray(length_profile(number_of, total, most, skew), jnp.int32)
    couples = (number_of - 1) // 2
    donor, receiver = tallies[1:1 + 2 * couples:2], tallies[2:2 + 2 * couples:2]
    slack = jnp.minimum(donor - 1, most - receiver)
    passed = jax.random.randint(jax.random.fold_in(stream_key, 1), (couples,), 0, 1 << 20) % (slack + 1)
    tallies = tallies.at[1:1 + 2 * couples:2].set(donor - passed).at[2:2 + 2 * couples:2].set(receiver + passed)
    return tallies[jax.random.permutation(jax.random.fold_in(stream_key, 2), number_of)]


def setup_inputs(seed: int = 0) -> dict:
    key_of = jax.random.split(jax.random.key(seed), 13)
    fill = jnp.clip(1.0 * jax.random.uniform(key_of[0], (NC, LINKS), jnp.float32) ** block_levels(key_of[0], (NC, LINKS), ((1, 32),), -0.2, 0.2), 0.0, 1.0)
    capacity = jnp.clip(jnp.exp(math.log(1.0) - 1.609438 * jax.random.uniform(key_of[1], (LINKS,), jnp.float32) ** block_levels(key_of[1], (LINKS,), ((0, 32),), -0.2, 0.2)), 0.2, 1.0)
    free_time = jnp.clip(jnp.exp(math.log(3.0) - 1.7917595 * jax.random.uniform(key_of[2], (LINKS,), jnp.float32) ** block_levels(key_of[2], (LINKS,), ((0, 32),), -0.2, 0.2)), 0.5, 3.0)
    split_share = jnp.clip(0.05 + 0.39999999 * jax.random.uniform(key_of[3], (2, LINKS), jnp.float32) ** block_levels(key_of[3], (2, LINKS), ((1, 32),), -0.2, 0.2), 0.05, 0.45)
    upstream_offset = with_ends(jax.random.randint(key_of[4], (2, LINKS), 0 - BND, BND + 1), jax.random.fold_in(key_of[4], 1), 0 - BND, BND).astype(jnp.int32)
    path_flow = jnp.clip(jnp.exp(math.log(0.1) - 2.3025851 * jax.random.uniform(key_of[5], (PATHS,), jnp.float32) ** block_levels(key_of[5], (PATHS,), ((0, 32),), -0.2, 0.2)), 0.01, 0.1)
    anchor = with_ends(jax.random.randint(key_of[6], (PATHS,), 0, LINK_DEV * N_ROUTE), jax.random.fold_in(key_of[6], 1), 0, (LINK_DEV * N_ROUTE) - 1).astype(jnp.int32)
    depart = with_ends(jax.random.randint(key_of[7], (PATHS,), 0, NI), jax.random.fold_in(key_of[7], 1), 0, NI - 1).astype(jnp.int32)
    od_pair = jax.vmap(lambda own: jnp.searchsorted(jnp.cumsum(ragged_sizes(own, ODS_DEV, PATH_DEV, OD_MOST, 0)), jnp.arange(PATH_DEV), side="right"))(jax.random.split(key_of[8], BLOCKS)).reshape((BLOCKS, PATH_DEV)).astype(jnp.int32)
    swap_rate = with_ends(jax.random.randint(key_of[9], (BLOCKS, ODS_DEV), 1, 9), jax.random.fold_in(key_of[9], 1), 1, 8).astype(jnp.int32)
    tile_index = draw_tile_index(jax.random.fold_in(key_of[12], 71), 0)
    incidence = draw_incidence(jax.random.fold_in(key_of[12], 71), 0)
    return {"fill": fill, "capacity": capacity, "free_time": free_time, "split_share": split_share, "upstream_offset": upstream_offset, "path_flow": path_flow, "anchor": anchor, "depart": depart, "od_pair": od_pair, "swap_rate": swap_rate, "tile_index": tile_index, "incidence": incidence}


def sweep(state, capacity):
    rho = state[:NC]
    queue = state[NC]
    jam = 4.0 * capacity
    send = jnp.minimum(rho, capacity)
    recv = jnp.minimum(capacity, 0.5 * (jam - rho))
    inner = jnp.minimum(send[:-1], recv[1:])
    outflow = send[NC - 1]
    return rho, queue, recv, inner, outflow


def finish(rho, queue, recv, inner, outflow, arriving):
    waiting = queue + arriving
    entering = jnp.minimum(waiting, recv[0])
    queue = waiting - entering
    into = jnp.concatenate([entering[None], inner], 0)
    leaving = jnp.concatenate([inner, outflow[None]], 0)
    rho = rho + into - leaving
    return jnp.concatenate([rho, queue[None]], 0)


def occupy(state, capacity):
    return (jnp.sum(state[:NC], 0) + state[NC]) / capacity


def group_min(cost, group):
    reach = OD_MOST - 1
    count = cost.shape[0]
    padded_cost = jnp.pad(cost, reach, constant_values=1e30)
    padded_group = jnp.pad(group, reach, constant_values=-1)
    best = cost
    for shift in range(2 * reach + 1):
        near_cost = padded_cost[shift:shift + count]
        near_group = padded_group[shift:shift + count]
        best = jnp.minimum(best, jnp.where(near_group == group, near_cost, best))
    return best


def swap_flows(cost, flow, group, rate_num):
    best = group_min(cost, group)
    rate = jnp.take(rate_num, group).astype(jnp.float32) / 16.0
    moved = rate * flow * (cost - best) / cost
    pull = (best / cost) ** 4
    moved_sum = jax.ops.segment_sum(moved, group, num_segments=rate_num.shape[0])
    pull_sum = jax.ops.segment_sum(pull, group, num_segments=rate_num.shape[0])
    return flow - moved + jnp.take(moved_sum, group) * pull / jnp.take(pull_sum, group)


def select_depart(totals, depart_tile):
    levels = jnp.arange(totals.shape[1], dtype=jnp.int32)
    chosen = jnp.where(levels[None, :, None] == depart_tile[:, None, :], totals, 0.0)
    return jnp.sum(chosen, 1)


def reference(fill, capacity, free_time, split_share, upstream_offset, path_flow, anchor, depart, od_pair, swap_rate, tile_index, incidence):
    paths = jnp.arange(PATHS, dtype=jnp.int32)
    region = paths // (PATH_DEV * N_ROUTE)
    target = (region * (LINK_DEV * N_ROUTE) + anchor).astype(jnp.int32)
    entry = jax.ops.segment_sum(path_flow, target, num_segments=LINKS)
    links = jnp.arange(LINKS, dtype=jnp.int32)
    up_first = (links + upstream_offset[0]) % LINKS
    up_second = (links + upstream_offset[1]) % LINKS
    state = jnp.concatenate([fill * (4.0 * capacity), jnp.zeros((1, LINKS), jnp.float32)], 0)

    def one_step(state, unused):
        rho, queue, recv, inner, outflow = sweep(state, capacity)
        arriving = entry + split_share[0] * outflow[up_first] + split_share[1] * outflow[up_second]
        state = finish(rho, queue, recv, inner, outflow, arriving)
        return state, occupy(state, capacity)

    def one_interval(state, unused):
        state, occupancy = lax.scan(one_step, state, None, length=ISTEPS)
        return state, free_time + jnp.sum(occupancy, 0) / ISTEPS

    state, costs = lax.scan(one_interval, state, None, length=NI)
    link_cost = costs.astype(jnp.bfloat16)
    tiles = link_cost.reshape(NI, LINKS // 128, 128).transpose(1, 0, 2)

    def block_cost(args):
        names, shares = args
        fetched = tiles[names]
        return jnp.einsum("ptil,ptlq->piq", fetched.astype(jnp.float32), shares.astype(jnp.float32))

    totals = lax.map(block_cost, (tile_index.reshape(BLOCKS, PTILE_DEV, TPT), incidence.reshape(BLOCKS, PTILE_DEV, TPT, 128, 128)))
    totals = totals.reshape(PTILES, NI, 128)
    path_cost = select_depart(totals, depart.reshape(PTILES, 128)).reshape(PATHS) / 256.0
    cost_rows = path_cost.reshape(BLOCKS, PATH_DEV)
    flow_rows = path_flow.reshape(BLOCKS, PATH_DEV)
    new_flow = jax.vmap(swap_flows)(cost_rows, flow_rows, od_pair, swap_rate).reshape(PATHS)
    return state[:NC], path_cost, new_flow
```

```python
import jax
import jax.numpy as jnp
from jax import lax
from jax.experimental import pallas as pl
from jax.experimental.pallas import tpu as pltpu
from jax.sharding import PartitionSpec as P

NC = 4
BND = 32
ISTEPS = 5
NI = 12
OD_MOST = 8
LINE = ("region", "route")


def halo_width(span):
    width = NI * ISTEPS * BND
    while (span + 2 * width) % 1024:
        width += 1
    return width


def padded(cells, width):
    count = lax.axis_size(LINE)
    head = cells[:, :width]
    tail = cells[:, cells.shape[1] - width :]
    return jnp.concatenate(
        [
            lax.ppermute(tail, LINE, [(i, (i + 1) % count) for i in range(count)]),
            cells,
            lax.ppermute(head, LINE, [((i + 1) % count, i) for i in range(count)]),
        ],
        axis=1,
    )


def to_cols(rows):
    extent = rows.shape[-1]
    lead = rows.shape[:-1]
    return jnp.swapaxes(rows.reshape(lead + (128, extent // 128)), -1, -2)


def from_cols(cols):
    lead = cols.shape[:-2]
    return jnp.swapaxes(cols, -1, -2).reshape(lead + (-1,))


def sim_kernel(st0_ref, cons_ref, occ_ref, st_ref, w_ref, p_ref):
    rows = st0_ref.shape[1]
    st_ref[...] = st0_ref[...]
    s0 = cons_ref[1]
    s1 = cons_ref[2]
    o0 = cons_ref[3]
    o1 = cons_ref[4]
    for k in range(2 * BND + 1):
        d = float(k - BND)
        w_ref[k] = jnp.where(o0 == d, s0, 0.0) + jnp.where(o1 == d, s1, 0.0)

    def step(j, acc):
        cap = cons_ref[0]
        jam = 4.0 * cap
        rho = [st_ref[c] for c in range(NC)]
        queue = st_ref[NC]
        send = [jnp.minimum(r, cap) for r in rho]
        recv = [jnp.minimum(cap, 0.5 * (jam - r)) for r in rho]
        inner = [jnp.minimum(send[c], recv[c + 1]) for c in range(NC - 1)]
        outflow = send[NC - 1]
        p_ref[BND : BND + rows] = outflow
        p_ref[BND + rows :] = pltpu.roll(outflow[:BND], 127, 1)
        p_ref[:BND] = pltpu.roll(outflow[rows - BND :], 1, 1)
        arriving = cons_ref[5]
        for k in range(2 * BND + 1):
            arriving = arriving + w_ref[k] * p_ref[pl.ds(k, rows), :]
        waiting = queue + arriving
        entering = jnp.minimum(waiting, recv[0])
        queue = waiting - entering
        into = [entering] + inner
        leaving = inner + [outflow]
        new = [(rho[c] + into[c]) - leaving[c] for c in range(NC)]
        for c in range(NC):
            st_ref[c] = new[c]
        st_ref[NC] = queue
        occ = ((((new[0] + new[1]) + new[2]) + new[3]) + queue) / cap
        return acc + occ

    def interval(i, carry):
        acc = lax.fori_loop(0, ISTEPS, step, jnp.zeros((rows, 128), jnp.float32))
        occ_ref[i] = acc
        return carry

    lax.fori_loop(0, occ_ref.shape[0], interval, 0)


def simulate(st0, cons, count):
    rows = st0.shape[1]
    return pl.pallas_call(
        sim_kernel,
        out_shape=(
            jax.ShapeDtypeStruct((count, rows, 128), jnp.float32),
            jax.ShapeDtypeStruct(st0.shape, jnp.float32),
        ),
        scratch_shapes=[
            pltpu.VMEM((2 * BND + 1, rows, 128), jnp.float32),
            pltpu.VMEM((rows + 2 * BND, 128), jnp.float32),
        ],
    )(st0, cons)


def group_min(cost, group):
    reach = OD_MOST - 1
    count = cost.shape[0]
    padded_cost = jnp.pad(cost, reach, constant_values=1e30)
    padded_group = jnp.pad(group, reach, constant_values=-1)
    best = cost
    for shift in range(2 * reach + 1):
        near_cost = padded_cost[shift : shift + count]
        near_group = padded_group[shift : shift + count]
        best = jnp.minimum(best, jnp.where(near_group == group, near_cost, best))
    return best


def group_sum(values, group):
    reach = OD_MOST - 1
    count = values.shape[0]
    padded_values = jnp.pad(values, reach)
    padded_group = jnp.pad(group, reach, constant_values=-1)
    total = jnp.zeros_like(values)
    for shift in range(2 * reach + 1):
        near_values = padded_values[shift : shift + count]
        near_group = padded_group[shift : shift + count]
        total = total + jnp.where(near_group == group, near_values, 0.0)
    return total


def swap_flows(cost, flow, group, rate_num):
    best = group_min(cost, group)
    rate = jnp.take(rate_num, group).astype(jnp.float32) / 16.0
    moved = rate * flow * (cost - best) / cost
    pull = (best / cost) ** 4
    return flow - moved + group_sum(moved, group) * pull / group_sum(pull, group)


def select_depart(totals, depart_tile):
    levels = jnp.arange(totals.shape[1], dtype=jnp.int32)
    chosen = jnp.where(levels[None, :, None] == depart_tile[:, None, :], totals, 0.0)
    return jnp.sum(chosen, 1)


def body(
    fill,
    capacity,
    free_time,
    split_share,
    upstream_offset,
    path_flow,
    anchor,
    depart,
    od_pair,
    swap_rate,
    tile_index,
    incidence,
):
    span = fill.shape[1]
    region_links = span * lax.axis_size("route")
    link_tiles = jnp.arange(region_links // 128, dtype=jnp.int32)
    lanes = jnp.arange(128, dtype=jnp.int32)
    tile_pick = jnp.where((anchor // 128)[None, :] == link_tiles[:, None], path_flow[None, :], 0.0)
    lane_pick = ((anchor % 128)[:, None] == lanes[None, :]).astype(jnp.float32)
    local_entry = jnp.dot(
        tile_pick, lane_pick, precision=lax.Precision.HIGHEST, preferred_element_type=jnp.float32
    ).reshape(-1)
    entry = lax.psum_scatter(local_entry, "route", scatter_dimension=0, tiled=True)

    width = halo_width(span)
    rows_in = jnp.concatenate(
        [fill, capacity[None], split_share, upstream_offset.astype(jnp.float32), entry[None]], 0
    )
    wide = padded(rows_in, width)
    wide_cap = wide[NC]
    st0 = jnp.concatenate([wide[:NC] * (4.0 * wide_cap), jnp.zeros_like(wide[:1])], 0)
    cons = wide[NC:]
    occ, state = simulate(to_cols(st0), to_cols(cons), NI)
    occ = from_cols(occ)[:, width : width + span]
    state = from_cols(state)[:NC, width : width + span]
    costs = free_time + occ / ISTEPS

    link_cost = costs.astype(jnp.bfloat16)
    tiles = link_cost.reshape(NI, span // 128, 128).transpose(1, 0, 2)
    wanted_tiles = tile_index.reshape(-1)
    every_tile = lax.all_gather(tiles, LINE, axis=0, tiled=True)
    fetched = every_tile[wanted_tiles]
    fetched = fetched.reshape(tile_index.shape[0], tile_index.shape[1], NI, 128)
    totals = jnp.einsum("ptil,ptlq->piq", fetched, incidence, preferred_element_type=jnp.float32)
    path_cost = select_depart(totals, depart.reshape(-1, 128)).reshape(-1) / 256.0
    new_flow = swap_flows(path_cost, path_flow, od_pair[0], swap_rate[0])
    return (state, path_cost, new_flow)


def solution(mesh):
    return jax.shard_map(
        body,
        mesh=mesh,
        in_specs=(
            P(None, LINE),
            P(LINE),
            P(LINE),
            P(None, LINE),
            P(None, LINE),
            P(LINE),
            P(LINE),
            P(LINE),
            P(LINE, None),
            P(LINE, None),
            P(LINE, None),
            P(LINE, None, None, None),
        ),
        out_specs=(P(None, LINE), P(LINE), P(LINE)),
        check_vma=False,
    )
```

```python
import jax
import jax.numpy as jnp
from jax import lax
from jax.experimental import pallas as pl
from jax.experimental.pallas import tpu as pltpu
from jax.sharding import PartitionSpec as P

NC = 4
BND = 32
ISTEPS = 5
NI = 12
OD_MOST = 8
LINE = ("z", "plane", "route")


def halo_width(span):
    width = NI * ISTEPS * BND
    while (span + 2 * width) % 1024:
        width += 1
    return width


def padded(cells, width):
    count = lax.axis_size(LINE)
    head = cells[:, :width]
    tail = cells[:, cells.shape[1] - width :]
    return jnp.concatenate(
        [
            lax.ppermute(tail, LINE, [(i, (i + 1) % count) for i in range(count)]),
            cells,
            lax.ppermute(head, LINE, [((i + 1) % count, i) for i in range(count)]),
        ],
        axis=1,
    )


def to_cols(rows):
    extent = rows.shape[-1]
    lead = rows.shape[:-1]
    return jnp.swapaxes(rows.reshape(lead + (128, extent // 128)), -1, -2)


def from_cols(cols):
    lead = cols.shape[:-2]
    return jnp.swapaxes(cols, -1, -2).reshape(lead + (-1,))


def sim_kernel(st0_ref, cons_ref, occ_ref, st_ref, w_ref, p_ref):
    rows = st0_ref.shape[1]
    st_ref[...] = st0_ref[...]
    s0 = cons_ref[1]
    s1 = cons_ref[2]
    o0 = cons_ref[3]
    o1 = cons_ref[4]
    for k in range(2 * BND + 1):
        d = float(k - BND)
        w_ref[k] = jnp.where(o0 == d, s0, 0.0) + jnp.where(o1 == d, s1, 0.0)

    def step(j, acc):
        cap = cons_ref[0]
        jam = 4.0 * cap
        rho = [st_ref[c] for c in range(NC)]
        queue = st_ref[NC]
        send = [jnp.minimum(r, cap) for r in rho]
        recv = [jnp.minimum(cap, 0.5 * (jam - r)) for r in rho]
        inner = [jnp.minimum(send[c], recv[c + 1]) for c in range(NC - 1)]
        outflow = send[NC - 1]
        p_ref[BND : BND + rows] = outflow
        p_ref[BND + rows :] = pltpu.roll(outflow[:BND], 127, 1)
        p_ref[:BND] = pltpu.roll(outflow[rows - BND :], 1, 1)
        arriving = cons_ref[5]
        for k in range(2 * BND + 1):
            arriving = arriving + w_ref[k] * p_ref[pl.ds(k, rows), :]
        waiting = queue + arriving
        entering = jnp.minimum(waiting, recv[0])
        queue = waiting - entering
        into = [entering] + inner
        leaving = inner + [outflow]
        new = [(rho[c] + into[c]) - leaving[c] for c in range(NC)]
        for c in range(NC):
            st_ref[c] = new[c]
        st_ref[NC] = queue
        occ = ((((new[0] + new[1]) + new[2]) + new[3]) + queue) / cap
        return acc + occ

    def interval(i, carry):
        acc = lax.fori_loop(0, ISTEPS, step, jnp.zeros((rows, 128), jnp.float32))
        occ_ref[i] = acc
        return carry

    lax.fori_loop(0, occ_ref.shape[0], interval, 0)


def simulate(st0, cons, count):
    rows = st0.shape[1]
    return pl.pallas_call(
        sim_kernel,
        out_shape=(
            jax.ShapeDtypeStruct((count, rows, 128), jnp.float32),
            jax.ShapeDtypeStruct(st0.shape, jnp.float32),
        ),
        scratch_shapes=[
            pltpu.VMEM((2 * BND + 1, rows, 128), jnp.float32),
            pltpu.VMEM((rows + 2 * BND, 128), jnp.float32),
        ],
    )(st0, cons)


def group_min(cost, group):
    reach = OD_MOST - 1
    count = cost.shape[0]
    padded_cost = jnp.pad(cost, reach, constant_values=1e30)
    padded_group = jnp.pad(group, reach, constant_values=-1)
    best = cost
    for shift in range(2 * reach + 1):
        near_cost = padded_cost[shift : shift + count]
        near_group = padded_group[shift : shift + count]
        best = jnp.minimum(best, jnp.where(near_group == group, near_cost, best))
    return best


def group_sum(values, group):
    reach = OD_MOST - 1
    count = values.shape[0]
    padded_values = jnp.pad(values, reach)
    padded_group = jnp.pad(group, reach, constant_values=-1)
    total = jnp.zeros_like(values)
    for shift in range(2 * reach + 1):
        near_values = padded_values[shift : shift + count]
        near_group = padded_group[shift : shift + count]
        total = total + jnp.where(near_group == group, near_values, 0.0)
    return total


def pick_rate(rate_num, group):
    count = rate_num.shape[0]
    table = rate_num.reshape(count // 128, 128).astype(jnp.float32)
    row_pick = ((group // 128)[:, None] == jnp.arange(count // 128)[None, :]).astype(jnp.float32)
    picked = jnp.dot(row_pick, table, precision=lax.Precision.HIGHEST, preferred_element_type=jnp.float32)
    lanes = jnp.arange(128, dtype=jnp.int32)
    return jnp.sum(jnp.where((group % 128)[:, None] == lanes[None, :], picked, 0.0), axis=1)


def swap_flows(cost, flow, group, rate_num):
    best = group_min(cost, group)
    rate = pick_rate(rate_num, group) / 16.0
    moved = rate * flow * (cost - best) / cost
    pull = (best / cost) ** 4
    return flow - moved + group_sum(moved, group) * pull / group_sum(pull, group)


def select_depart(totals, depart_tile):
    levels = jnp.arange(totals.shape[1], dtype=jnp.int32)
    chosen = jnp.where(levels[None, :, None] == depart_tile[:, None, :], totals, 0.0)
    return jnp.sum(chosen, 1)


def body(
    fill,
    capacity,
    free_time,
    split_share,
    upstream_offset,
    path_flow,
    anchor,
    depart,
    od_pair,
    swap_rate,
    tile_index,
    incidence,
):
    span = fill.shape[1]
    region_links = span * lax.axis_size("route")
    link_tiles = jnp.arange(region_links // 128, dtype=jnp.int32)
    lanes = jnp.arange(128, dtype=jnp.int32)
    tile_pick = jnp.where((anchor // 128)[None, :] == link_tiles[:, None], path_flow[None, :], 0.0)
    lane_pick = ((anchor % 128)[:, None] == lanes[None, :]).astype(jnp.float32)
    local_entry = jnp.dot(
        tile_pick, lane_pick, precision=lax.Precision.HIGHEST, preferred_element_type=jnp.float32
    ).reshape(-1)
    entry = lax.psum_scatter(local_entry, "route", scatter_dimension=0, tiled=True)

    width = halo_width(span)
    rows_in = jnp.concatenate(
        [fill, capacity[None], split_share, upstream_offset.astype(jnp.float32), entry[None]], 0
    )
    wide = padded(rows_in, width)
    wide_cap = wide[NC]
    st0 = jnp.concatenate([wide[:NC] * (4.0 * wide_cap), jnp.zeros_like(wide[:1])], 0)
    cons = wide[NC:]
    occ, state = simulate(to_cols(st0), to_cols(cons), NI)
    occ = from_cols(occ)[:, width : width + span]
    state = from_cols(state)[:NC, width : width + span]
    costs = free_time + occ / ISTEPS

    link_cost = costs.astype(jnp.bfloat16)
    tiles = link_cost.reshape(NI, span // 128, 128).transpose(1, 0, 2)
    wanted_tiles = tile_index.reshape(-1)
    every_tile = lax.all_gather(tiles, ("plane", "route"), axis=0, tiled=True)
    every_tile = lax.all_gather(every_tile, "z", axis=0, tiled=True)
    fetched = every_tile[wanted_tiles]
    fetched = fetched.reshape(tile_index.shape[0], tile_index.shape[1], NI, 128)
    totals = jnp.einsum("ptil,ptlq->piq", fetched, incidence, preferred_element_type=jnp.float32)
    path_cost = select_depart(totals, depart.reshape(-1, 128)).reshape(-1) / 256.0
    new_flow = swap_flows(path_cost, path_flow, od_pair[0], swap_rate[0])
    return (state, path_cost, new_flow)


def z_count(devices):
    try:
        return len({d.coords[2] for d in devices.flat})
    except (AttributeError, IndexError, TypeError):
        return 4


def solution(mesh):
    devices = mesh.devices
    count = z_count(devices)
    split = jax.sharding.Mesh(
        devices.reshape(count, devices.shape[0] // count, devices.shape[1]), LINE
    )
    return jax.shard_map(
        body,
        mesh=split,
        in_specs=(
            P(None, LINE),
            P(LINE),
            P(LINE),
            P(None, LINE),
            P(None, LINE),
            P(LINE),
            P(LINE),
            P(LINE),
            P(LINE, None),
            P(LINE, None),
            P(LINE, None),
            P(LINE, None, None, None),
        ),
        out_specs=(P(None, LINE), P(LINE), P(LINE)),
        check_vma=False,
    )
```

```python
import jax
import jax.numpy as jnp
from jax import lax
from jax.experimental import pallas as pl
from jax.experimental.pallas import tpu as pltpu
from jax.sharding import PartitionSpec as P

NC = 4
BND = 32
ISTEPS = 5
NI = 12
OD_MOST = 8
LINE = ("z", "plane", "route")


def halo_width(span):
    width = NI * ISTEPS * BND
    while (span + 2 * width) % 1024:
        width += 1
    return width


def padded(cells, width):
    count = lax.axis_size(LINE)
    head = cells[:, :width]
    tail = cells[:, cells.shape[1] - width :]
    return jnp.concatenate(
        [
            lax.ppermute(tail, LINE, [(i, (i + 1) % count) for i in range(count)]),
            cells,
            lax.ppermute(head, LINE, [((i + 1) % count, i) for i in range(count)]),
        ],
        axis=1,
    )


def to_cols(rows):
    extent = rows.shape[-1]
    lead = rows.shape[:-1]
    return jnp.swapaxes(rows.reshape(lead + (128, extent // 128)), -1, -2)


def from_cols(cols):
    lead = cols.shape[:-2]
    return jnp.swapaxes(cols, -1, -2).reshape(lead + (-1,))


def sim_kernel(st0_ref, cons_ref, occ_ref, st_ref, w_ref, p_ref):
    rows = st0_ref.shape[1]
    st_ref[...] = st0_ref[...]
    s0 = cons_ref[1]
    s1 = cons_ref[2]
    o0 = cons_ref[3]
    o1 = cons_ref[4]
    for k in range(2 * BND + 1):
        d = float(k - BND)
        w_ref[k] = jnp.where(o0 == d, s0, 0.0) + jnp.where(o1 == d, s1, 0.0)

    def step(j, acc):
        cap = cons_ref[0]
        jam = 4.0 * cap
        rho = [st_ref[c] for c in range(NC)]
        queue = st_ref[NC]
        send = [jnp.minimum(r, cap) for r in rho]
        recv = [jnp.minimum(cap, 0.5 * (jam - r)) for r in rho]
        inner = [jnp.minimum(send[c], recv[c + 1]) for c in range(NC - 1)]
        outflow = send[NC - 1]
        p_ref[BND : BND + rows] = outflow
        p_ref[BND + rows :] = pltpu.roll(outflow[:BND], 127, 1)
        p_ref[:BND] = pltpu.roll(outflow[rows - BND :], 1, 1)
        arriving = cons_ref[5]
        for k in range(2 * BND + 1):
            arriving = arriving + w_ref[k] * p_ref[pl.ds(k, rows), :]
        waiting = queue + arriving
        entering = jnp.minimum(waiting, recv[0])
        queue = waiting - entering
        into = [entering] + inner
        leaving = inner + [outflow]
        new = [(rho[c] + into[c]) - leaving[c] for c in range(NC)]
        for c in range(NC):
            st_ref[c] = new[c]
        st_ref[NC] = queue
        occ = ((((new[0] + new[1]) + new[2]) + new[3]) + queue) / cap
        return acc + occ

    def interval(i, carry):
        acc = lax.fori_loop(0, ISTEPS, step, jnp.zeros((rows, 128), jnp.float32))
        occ_ref[i] = acc
        return carry

    lax.fori_loop(0, occ_ref.shape[0], interval, 0)


def simulate(st0, cons, count):
    rows = st0.shape[1]
    return pl.pallas_call(
        sim_kernel,
        out_shape=(
            jax.ShapeDtypeStruct((count, rows, 128), jnp.float32),
            jax.ShapeDtypeStruct(st0.shape, jnp.float32),
        ),
        scratch_shapes=[
            pltpu.VMEM((2 * BND + 1, rows, 128), jnp.float32),
            pltpu.VMEM((rows + 2 * BND, 128), jnp.float32),
        ],
    )(st0, cons)


def group_min(cost, group):
    reach = OD_MOST - 1
    count = cost.shape[0]
    padded_cost = jnp.pad(cost, reach, constant_values=1e30)
    padded_group = jnp.pad(group, reach, constant_values=-1)
    best = cost
    for shift in range(2 * reach + 1):
        near_cost = padded_cost[shift : shift + count]
        near_group = padded_group[shift : shift + count]
        best = jnp.minimum(best, jnp.where(near_group == group, near_cost, best))
    return best


def group_sum(values, group):
    reach = OD_MOST - 1
    count = values.shape[0]
    padded_values = jnp.pad(values, reach)
    padded_group = jnp.pad(group, reach, constant_values=-1)
    total = jnp.zeros_like(values)
    for shift in range(2 * reach + 1):
        near_values = padded_values[shift : shift + count]
        near_group = padded_group[shift : shift + count]
        total = total + jnp.where(near_group == group, near_values, 0.0)
    return total


def pick_rate(rate_num, group):
    count = rate_num.shape[0]
    table = rate_num.reshape(count // 128, 128).astype(jnp.float32)
    row_pick = ((group // 128)[:, None] == jnp.arange(count // 128)[None, :]).astype(jnp.float32)
    picked = jnp.dot(row_pick, table, precision=lax.Precision.HIGHEST, preferred_element_type=jnp.float32)
    lanes = jnp.arange(128, dtype=jnp.int32)
    return jnp.sum(jnp.where((group % 128)[:, None] == lanes[None, :], picked, 0.0), axis=1)


def swap_flows(cost, flow, group, rate):
    best = group_min(cost, group)
    moved = rate * flow * (cost - best) / cost
    pull = (best / cost) ** 4
    return flow - moved + group_sum(moved, group) * pull / group_sum(pull, group)


def select_depart(totals, depart_tile):
    levels = jnp.arange(totals.shape[1], dtype=jnp.int32)
    chosen = jnp.where(levels[None, :, None] == depart_tile[:, None, :], totals, 0.0)
    return jnp.sum(chosen, 1)


def body(
    fill,
    capacity,
    free_time,
    split_share,
    upstream_offset,
    path_flow,
    anchor,
    depart,
    od_pair,
    swap_rate,
    tile_index,
    incidence,
):
    span = fill.shape[1]
    region_links = span * lax.axis_size("route")
    link_tiles = jnp.arange(region_links // 128, dtype=jnp.int32)
    lanes = jnp.arange(128, dtype=jnp.int32)
    tile_pick = jnp.where((anchor // 128)[None, :] == link_tiles[:, None], path_flow[None, :], 0.0)
    lane_pick = ((anchor % 128)[:, None] == lanes[None, :]).astype(jnp.float32)
    local_entry = jnp.dot(
        tile_pick, lane_pick, precision=lax.Precision.HIGHEST, preferred_element_type=jnp.float32
    ).reshape(-1)
    entry = lax.psum_scatter(local_entry, "route", scatter_dimension=0, tiled=True)

    width = halo_width(span)
    rows_in = jnp.concatenate(
        [fill, capacity[None], split_share, upstream_offset.astype(jnp.float32), entry[None]], 0
    )
    wide = padded(rows_in, width)
    wide_cap = wide[NC]
    st0 = jnp.concatenate([wide[:NC] * (4.0 * wide_cap), jnp.zeros_like(wide[:1])], 0)
    cons = wide[NC:]
    occ, state = simulate(to_cols(st0), to_cols(cons), NI)
    occ = from_cols(occ)[:, width : width + span]
    state = from_cols(state)[:NC, width : width + span]
    costs = free_time + occ / ISTEPS

    link_cost = costs.astype(jnp.bfloat16)
    tiles = link_cost.reshape(NI, span // 128, 128).transpose(1, 0, 2).reshape(span // 128, NI * 128)
    wanted_tiles = tile_index.reshape(-1)
    rate = pick_rate(swap_rate[0], od_pair[0]) / 16.0
    every_tile = lax.all_gather(tiles, LINE, axis=0, tiled=True)
    fetched = every_tile[wanted_tiles]
    fetched = fetched.reshape(tile_index.shape[0], tile_index.shape[1], NI, 128)
    totals = jnp.einsum("ptil,ptlq->piq", fetched, incidence, preferred_element_type=jnp.float32)
    path_cost = select_depart(totals, depart.reshape(-1, 128)).reshape(-1) / 256.0
    new_flow = swap_flows(path_cost, path_flow, od_pair[0], rate)
    return (state, path_cost, new_flow)


def z_count(devices):
    try:
        return len({d.coords[2] for d in devices.flat})
    except (AttributeError, IndexError, TypeError):
        return 4


def solution(mesh):
    devices = mesh.devices
    count = z_count(devices)
    split = jax.sharding.Mesh(
        devices.reshape(count, devices.shape[0] // count, devices.shape[1]), LINE
    )
    return jax.shard_map(
        body,
        mesh=split,
        in_specs=(
            P(None, LINE),
            P(LINE),
            P(LINE),
            P(None, LINE),
            P(None, LINE),
            P(LINE),
            P(LINE),
            P(LINE),
            P(LINE, None),
            P(LINE, None),
            P(LINE, None),
            P(LINE, None, None, None),
        ),
        out_specs=(P(None, LINE), P(LINE), P(LINE)),
        check_vma=False,
    )
```

```python
import jax
import jax.numpy as jnp
from jax import lax
from jax.experimental import pallas as pl
from jax.experimental.pallas import tpu as pltpu
from jax.sharding import PartitionSpec as P

NC = 4
BND = 32
ISTEPS = 5
NI = 12
OD_MOST = 8
LINE = ("z", "plane", "route")


def halo_width(span):
    width = NI * ISTEPS * BND
    while (span + 2 * width) % 1024:
        width += 1
    return width


def padded(cells, width):
    count = lax.axis_size(LINE)
    head = cells[:, :width]
    tail = cells[:, cells.shape[1] - width :]
    return jnp.concatenate(
        [
            lax.ppermute(tail, LINE, [(i, (i + 1) % count) for i in range(count)]),
            cells,
            lax.ppermute(head, LINE, [((i + 1) % count, i) for i in range(count)]),
        ],
        axis=1,
    )


def to_cols(rows):
    extent = rows.shape[-1]
    lead = rows.shape[:-1]
    return jnp.swapaxes(rows.reshape(lead + (128, extent // 128)), -1, -2)


def from_cols(cols):
    lead = cols.shape[:-2]
    return jnp.swapaxes(cols, -1, -2).reshape(lead + (-1,))


def sim_kernel(st0_ref, cons_ref, occ_ref, st_ref, w_ref, p_ref):
    rows = st0_ref.shape[1]
    st_ref[...] = st0_ref[...]
    s0 = cons_ref[1]
    s1 = cons_ref[2]
    o0 = cons_ref[3]
    o1 = cons_ref[4]
    for k in range(2 * BND + 1):
        d = float(k - BND)
        w_ref[k] = jnp.where(o0 == d, s0, 0.0) + jnp.where(o1 == d, s1, 0.0)

    def step(j, acc):
        cap = cons_ref[0]
        jam = 4.0 * cap
        rho = [st_ref[c] for c in range(NC)]
        queue = st_ref[NC]
        send = [jnp.minimum(r, cap) for r in rho]
        recv = [jnp.minimum(cap, 0.5 * (jam - r)) for r in rho]
        inner = [jnp.minimum(send[c], recv[c + 1]) for c in range(NC - 1)]
        outflow = send[NC - 1]
        p_ref[BND : BND + rows] = outflow
        p_ref[BND + rows :] = pltpu.roll(outflow[:BND], 127, 1)
        p_ref[:BND] = pltpu.roll(outflow[rows - BND :], 1, 1)
        arriving = cons_ref[5]
        for k in range(2 * BND + 1):
            arriving = arriving + w_ref[k] * p_ref[pl.ds(k, rows), :]
        waiting = queue + arriving
        entering = jnp.minimum(waiting, recv[0])
        queue = waiting - entering
        into = [entering] + inner
        leaving = inner + [outflow]
        new = [(rho[c] + into[c]) - leaving[c] for c in range(NC)]
        for c in range(NC):
            st_ref[c] = new[c]
        st_ref[NC] = queue
        occ = ((((new[0] + new[1]) + new[2]) + new[3]) + queue) / cap
        return acc + occ

    def interval(i, carry):
        acc = lax.fori_loop(0, ISTEPS, step, jnp.zeros((rows, 128), jnp.float32))
        occ_ref[i] = acc
        return carry

    lax.fori_loop(0, occ_ref.shape[0], interval, 0)


def simulate(st0, cons, count):
    rows = st0.shape[1]
    return pl.pallas_call(
        sim_kernel,
        out_shape=(
            jax.ShapeDtypeStruct((count, rows, 128), jnp.float32),
            jax.ShapeDtypeStruct(st0.shape, jnp.float32),
        ),
        scratch_shapes=[
            pltpu.VMEM((2 * BND + 1, rows, 128), jnp.float32),
            pltpu.VMEM((rows + 2 * BND, 128), jnp.float32),
        ],
    )(st0, cons)


def group_min(cost, group):
    reach = OD_MOST - 1
    count = cost.shape[0]
    padded_cost = jnp.pad(cost, reach, constant_values=1e30)
    padded_group = jnp.pad(group, reach, constant_values=-1)
    best = cost
    for shift in range(2 * reach + 1):
        near_cost = padded_cost[shift : shift + count]
        near_group = padded_group[shift : shift + count]
        best = jnp.minimum(best, jnp.where(near_group == group, near_cost, best))
    return best


def group_sum(values, group):
    reach = OD_MOST - 1
    count = values.shape[0]
    padded_values = jnp.pad(values, reach)
    padded_group = jnp.pad(group, reach, constant_values=-1)
    total = jnp.zeros_like(values)
    for shift in range(2 * reach + 1):
        near_values = padded_values[shift : shift + count]
        near_group = padded_group[shift : shift + count]
        total = total + jnp.where(near_group == group, near_values, 0.0)
    return total


def pick_rate(rate_num, group):
    count = rate_num.shape[0]
    table = rate_num.reshape(count // 128, 128).astype(jnp.float32)
    row_pick = ((group // 128)[:, None] == jnp.arange(count // 128)[None, :]).astype(jnp.float32)
    picked = jnp.dot(row_pick, table, precision=lax.Precision.HIGHEST, preferred_element_type=jnp.float32)
    lanes = jnp.arange(128, dtype=jnp.int32)
    return jnp.sum(jnp.where((group % 128)[:, None] == lanes[None, :], picked, 0.0), axis=1)


def swap_flows(cost, flow, group, rate):
    best = group_min(cost, group)
    moved = rate * flow * (cost - best) / cost
    pull = (best / cost) ** 4
    return flow - moved + group_sum(moved, group) * pull / group_sum(pull, group)


def select_depart(totals, depart_tile):
    levels = jnp.arange(totals.shape[1], dtype=jnp.int32)
    chosen = jnp.where(levels[None, :, None] == depart_tile[:, None, :], totals, 0.0)
    return jnp.sum(chosen, 1)


def body(
    fill,
    capacity,
    free_time,
    split_share,
    upstream_offset,
    path_flow,
    anchor,
    depart,
    od_pair,
    swap_rate,
    tile_index,
    incidence,
):
    span = fill.shape[1]
    region_links = span * lax.axis_size("route")
    link_tiles = jnp.arange(region_links // 128, dtype=jnp.int32)
    lanes = jnp.arange(128, dtype=jnp.int32)
    tile_pick = jnp.where((anchor // 128)[None, :] == link_tiles[:, None], path_flow[None, :], 0.0)
    lane_pick = ((anchor % 128)[:, None] == lanes[None, :]).astype(jnp.float32)
    local_entry = jnp.dot(
        tile_pick, lane_pick, precision=lax.Precision.HIGHEST, preferred_element_type=jnp.float32
    ).reshape(-1)
    entry = lax.psum_scatter(local_entry, "route", scatter_dimension=0, tiled=True)

    width = halo_width(span)
    rows_in = jnp.concatenate(
        [fill, capacity[None], split_share, upstream_offset.astype(jnp.float32), entry[None]], 0
    )
    wide = padded(rows_in, width)
    wide_cap = wide[NC]
    st0 = jnp.concatenate([wide[:NC] * (4.0 * wide_cap), jnp.zeros_like(wide[:1])], 0)
    cons = wide[NC:]
    occ, state = simulate(to_cols(st0), to_cols(cons), NI)
    occ = from_cols(occ)[:, width : width + span]
    state = from_cols(state)[:NC, width : width + span]
    costs = free_time + occ / ISTEPS

    link_cost = costs.astype(jnp.bfloat16)
    tiles = link_cost.reshape(NI, span // 128, 128).transpose(1, 0, 2).reshape(span // 128, NI * 128)
    wanted_tiles = tile_index.reshape(-1)
    rate = pick_rate(swap_rate[0], od_pair[0]) / 16.0
    every_tile = lax.all_gather(tiles, "z", axis=0, tiled=True)
    piece = every_tile.shape[1] // 3
    every_tile = jnp.concatenate(
        [
            lax.all_gather(every_tile[:, c * piece : (c + 1) * piece], ("plane", "route"), axis=0, tiled=True)
            for c in range(3)
        ],
        1,
    )
    own = tiles.shape[0]
    planes = lax.axis_size(("plane", "route"))
    device = wanted_tiles // own
    wanted_tiles = (device % planes) * (lax.axis_size("z") * own) + (device // planes) * own + wanted_tiles % own
    fetched = every_tile[wanted_tiles]
    fetched = fetched.reshape(tile_index.shape[0], tile_index.shape[1], NI, 128)
    totals = jnp.einsum("ptil,ptlq->piq", fetched, incidence, preferred_element_type=jnp.float32)
    path_cost = select_depart(totals, depart.reshape(-1, 128)).reshape(-1) / 256.0
    new_flow = swap_flows(path_cost, path_flow, od_pair[0], rate)
    return (state, path_cost, new_flow)


def z_count(devices):
    try:
        return len({d.coords[2] for d in devices.flat})
    except (AttributeError, IndexError, TypeError):
        return 4


def solution(mesh):
    devices = mesh.devices
    count = z_count(devices)
    split = jax.sharding.Mesh(
        devices.reshape(count, devices.shape[0] // count, devices.shape[1]), LINE
    )
    return jax.shard_map(
        body,
        mesh=split,
        in_specs=(
            P(None, LINE),
            P(LINE),
            P(LINE),
            P(None, LINE),
            P(None, LINE),
            P(LINE),
            P(LINE),
            P(LINE),
            P(LINE, None),
            P(LINE, None),
            P(LINE, None),
            P(LINE, None, None, None),
        ),
        out_specs=(P(None, LINE), P(LINE), P(LINE)),
        check_vma=False,
    )
```

```python
import jax
import jax.numpy as jnp
from jax import lax
from jax.experimental import pallas as pl
from jax.experimental.pallas import tpu as pltpu
from jax.sharding import PartitionSpec as P

NC = 4
BND = 32
ISTEPS = 5
NI = 12
OD_MOST = 8
LINE = ("z", "plane", "route")


def halo_width(span):
    width = NI * ISTEPS * BND
    while (span + 2 * width) % 1024:
        width += 1
    return width


def padded(cells, width):
    count = lax.axis_size(LINE)
    head = cells[:, :width]
    tail = cells[:, cells.shape[1] - width :]
    return jnp.concatenate(
        [
            lax.ppermute(tail, LINE, [(i, (i + 1) % count) for i in range(count)]),
            cells,
            lax.ppermute(head, LINE, [((i + 1) % count, i) for i in range(count)]),
        ],
        axis=1,
    )


def entry_window(local_entry, span, width):
    count = lax.axis_size(LINE)
    owners = lax.axis_size("route")
    me = lax.axis_index(LINE)
    part = local_entry.reshape(owners, span)

    def chunk(device):
        row = lax.dynamic_index_in_dim(part, device % owners, 0, keepdims=False)
        return jnp.where(device // owners == me // owners, row, 0.0)

    total = None
    for k in range(-owners, owners + 1):
        target = (me - k) % count
        message = jnp.concatenate(
            [
                chunk((target - 1) % count)[span - width :],
                chunk(target),
                chunk((target + 1) % count)[:width],
            ]
        )
        if k:
            message = lax.ppermute(message, LINE, [(j, (j - k) % count) for j in range(count)])
        total = message if total is None else total + message
    return total


def to_cols(rows):
    extent = rows.shape[-1]
    lead = rows.shape[:-1]
    return jnp.swapaxes(rows.reshape(lead + (128, extent // 128)), -1, -2)


def from_cols(cols):
    lead = cols.shape[:-2]
    return jnp.swapaxes(cols, -1, -2).reshape(lead + (-1,))


def sim_kernel(st0_ref, cons_ref, occ_ref, st_ref, w_ref, p_ref):
    rows = st0_ref.shape[1]
    st_ref[...] = st0_ref[...]
    s0 = cons_ref[1]
    s1 = cons_ref[2]
    o0 = cons_ref[3]
    o1 = cons_ref[4]
    for k in range(2 * BND + 1):
        d = float(k - BND)
        w_ref[k] = jnp.where(o0 == d, s0, 0.0) + jnp.where(o1 == d, s1, 0.0)

    def step(j, acc):
        cap = cons_ref[0]
        jam = 4.0 * cap
        rho = [st_ref[c] for c in range(NC)]
        queue = st_ref[NC]
        send = [jnp.minimum(r, cap) for r in rho]
        recv = [jnp.minimum(cap, 0.5 * (jam - r)) for r in rho]
        inner = [jnp.minimum(send[c], recv[c + 1]) for c in range(NC - 1)]
        outflow = send[NC - 1]
        p_ref[BND : BND + rows] = outflow
        p_ref[BND + rows :] = pltpu.roll(outflow[:BND], 127, 1)
        p_ref[:BND] = pltpu.roll(outflow[rows - BND :], 1, 1)
        arriving = cons_ref[5]
        for k in range(2 * BND + 1):
            arriving = arriving + w_ref[k] * p_ref[pl.ds(k, rows), :]
        waiting = queue + arriving
        entering = jnp.minimum(waiting, recv[0])
        queue = waiting - entering
        into = [entering] + inner
        leaving = inner + [outflow]
        new = [(rho[c] + into[c]) - leaving[c] for c in range(NC)]
        for c in range(NC):
            st_ref[c] = new[c]
        st_ref[NC] = queue
        occ = ((((new[0] + new[1]) + new[2]) + new[3]) + queue) / cap
        return acc + occ

    def interval(i, carry):
        acc = lax.fori_loop(0, ISTEPS, step, jnp.zeros((rows, 128), jnp.float32))
        occ_ref[i] = acc
        return carry

    lax.fori_loop(0, occ_ref.shape[0], interval, 0)


def simulate(st0, cons, count):
    rows = st0.shape[1]
    return pl.pallas_call(
        sim_kernel,
        out_shape=(
            jax.ShapeDtypeStruct((count, rows, 128), jnp.float32),
            jax.ShapeDtypeStruct(st0.shape, jnp.float32),
        ),
        scratch_shapes=[
            pltpu.VMEM((2 * BND + 1, rows, 128), jnp.float32),
            pltpu.VMEM((rows + 2 * BND, 128), jnp.float32),
        ],
    )(st0, cons)


def group_min(cost, group):
    reach = OD_MOST - 1
    count = cost.shape[0]
    padded_cost = jnp.pad(cost, reach, constant_values=1e30)
    padded_group = jnp.pad(group, reach, constant_values=-1)
    best = cost
    for shift in range(2 * reach + 1):
        near_cost = padded_cost[shift : shift + count]
        near_group = padded_group[shift : shift + count]
        best = jnp.minimum(best, jnp.where(near_group == group, near_cost, best))
    return best


def group_sum(values, group):
    reach = OD_MOST - 1
    count = values.shape[0]
    padded_values = jnp.pad(values, reach)
    padded_group = jnp.pad(group, reach, constant_values=-1)
    total = jnp.zeros_like(values)
    for shift in range(2 * reach + 1):
        near_values = padded_values[shift : shift + count]
        near_group = padded_group[shift : shift + count]
        total = total + jnp.where(near_group == group, near_values, 0.0)
    return total


def pick_rate(rate_num, group):
    count = rate_num.shape[0]
    table = rate_num.reshape(count // 128, 128).astype(jnp.float32)
    row_pick = ((group // 128)[:, None] == jnp.arange(count // 128)[None, :]).astype(jnp.float32)
    picked = jnp.dot(row_pick, table, precision=lax.Precision.HIGHEST, preferred_element_type=jnp.float32)
    lanes = jnp.arange(128, dtype=jnp.int32)
    return jnp.sum(jnp.where((group % 128)[:, None] == lanes[None, :], picked, 0.0), axis=1)


def swap_flows(cost, flow, group, rate):
    best = group_min(cost, group)
    moved = rate * flow * (cost - best) / cost
    pull = (best / cost) ** 4
    return flow - moved + group_sum(moved, group) * pull / group_sum(pull, group)


def select_depart(totals, depart_tile):
    levels = jnp.arange(totals.shape[1], dtype=jnp.int32)
    chosen = jnp.where(levels[None, :, None] == depart_tile[:, None, :], totals, 0.0)
    return jnp.sum(chosen, 1)


def body(
    fill,
    capacity,
    free_time,
    split_share,
    upstream_offset,
    path_flow,
    anchor,
    depart,
    od_pair,
    swap_rate,
    tile_index,
    incidence,
):
    span = fill.shape[1]
    region_links = span * lax.axis_size("route")
    link_tiles = jnp.arange(region_links // 128, dtype=jnp.int32)
    lanes = jnp.arange(128, dtype=jnp.int32)
    tile_pick = jnp.where((anchor // 128)[None, :] == link_tiles[:, None], path_flow[None, :], 0.0)
    lane_pick = ((anchor % 128)[:, None] == lanes[None, :]).astype(jnp.float32)
    local_entry = jnp.dot(
        tile_pick, lane_pick, precision=lax.Precision.HIGHEST, preferred_element_type=jnp.float32
    ).reshape(-1)
    width = halo_width(span)
    wide = jnp.concatenate(
        [padded(jnp.concatenate([fill, capacity[None], split_share, upstream_offset.astype(jnp.float32)], 0), width),
         entry_window(local_entry, span, width)[None]],
        0,
    )
    wide_cap = wide[NC]
    st0 = jnp.concatenate([wide[:NC] * (4.0 * wide_cap), jnp.zeros_like(wide[:1])], 0)
    cons = wide[NC:]
    occ, state = simulate(to_cols(st0), to_cols(cons), NI)
    occ = from_cols(occ)[:, width : width + span]
    state = from_cols(state)[:NC, width : width + span]
    costs = free_time + occ / ISTEPS

    link_cost = costs.astype(jnp.bfloat16)
    tiles = link_cost.reshape(NI, span // 128, 128).transpose(1, 0, 2).reshape(span // 128, NI * 128)
    wanted_tiles = tile_index.reshape(-1)
    rate = pick_rate(swap_rate[0], od_pair[0]) / 16.0
    every_tile = lax.all_gather(tiles, "z", axis=0, tiled=True)
    piece = every_tile.shape[1] // 3
    every_tile = jnp.concatenate(
        [
            lax.all_gather(every_tile[:, c * piece : (c + 1) * piece], ("plane", "route"), axis=0, tiled=True)
            for c in range(3)
        ],
        1,
    )
    own = tiles.shape[0]
    planes = lax.axis_size(("plane", "route"))
    device = wanted_tiles // own
    wanted_tiles = (device % planes) * (lax.axis_size("z") * own) + (device // planes) * own + wanted_tiles % own
    fetched = every_tile[wanted_tiles]
    fetched = fetched.reshape(tile_index.shape[0], tile_index.shape[1], NI, 128)
    totals = jnp.einsum("ptil,ptlq->piq", fetched, incidence, preferred_element_type=jnp.float32)
    path_cost = select_depart(totals, depart.reshape(-1, 128)).reshape(-1) / 256.0
    new_flow = swap_flows(path_cost, path_flow, od_pair[0], rate)
    return (state, path_cost, new_flow)


def z_count(devices):
    try:
        return len({d.coords[2] for d in devices.flat})
    except (AttributeError, IndexError, TypeError):
        return 4


def solution(mesh):
    devices = mesh.devices
    count = z_count(devices)
    split = jax.sharding.Mesh(
        devices.reshape(count, devices.shape[0] // count, devices.shape[1]), LINE
    )
    return jax.shard_map(
        body,
        mesh=split,
        in_specs=(
            P(None, LINE),
            P(LINE),
            P(LINE),
            P(None, LINE),
            P(None, LINE),
            P(LINE),
            P(LINE),
            P(LINE),
            P(LINE, None),
            P(LINE, None),
            P(LINE, None),
            P(LINE, None, None, None),
        ),
        out_specs=(P(None, LINE), P(LINE), P(LINE)),
        check_vma=False,
    )
```

```python
import jax
import jax.numpy as jnp
from jax import lax
from jax.experimental import pallas as pl
from jax.experimental.pallas import tpu as pltpu
from jax.sharding import PartitionSpec as P

NC = 4
BND = 32
ISTEPS = 5
NI = 12
OD_MOST = 8
LINE = ("z", "plane", "route")


def halo_width(span):
    width = NI * ISTEPS * BND
    while (span + 2 * width) % 1024:
        width += 1
    return width


def padded(cells, width):
    count = lax.axis_size(LINE)
    head = cells[:, :width]
    tail = cells[:, cells.shape[1] - width :]
    return jnp.concatenate(
        [
            lax.ppermute(tail, LINE, [(i, (i + 1) % count) for i in range(count)]),
            cells,
            lax.ppermute(head, LINE, [((i + 1) % count, i) for i in range(count)]),
        ],
        axis=1,
    )


def to_cols(rows):
    extent = rows.shape[-1]
    lead = rows.shape[:-1]
    return jnp.swapaxes(rows.reshape(lead + (128, extent // 128)), -1, -2)


def from_cols(cols):
    lead = cols.shape[:-2]
    return jnp.swapaxes(cols, -1, -2).reshape(lead + (-1,))


def sim_kernel(st0_ref, cons_ref, occ_ref, st_ref, w_ref, p_ref):
    rows = st0_ref.shape[1]
    st_ref[...] = st0_ref[...]
    s0 = cons_ref[1]
    s1 = cons_ref[2]
    o0 = cons_ref[3]
    o1 = cons_ref[4]
    for k in range(2 * BND + 1):
        d = float(k - BND)
        w_ref[k] = jnp.where(o0 == d, s0, 0.0) + jnp.where(o1 == d, s1, 0.0)

    def step(j, acc):
        cap = cons_ref[0]
        jam = 4.0 * cap
        rho = [st_ref[c] for c in range(NC)]
        queue = st_ref[NC]
        send = [jnp.minimum(r, cap) for r in rho]
        recv = [jnp.minimum(cap, 0.5 * (jam - r)) for r in rho]
        inner = [jnp.minimum(send[c], recv[c + 1]) for c in range(NC - 1)]
        outflow = send[NC - 1]
        p_ref[BND : BND + rows] = outflow
        p_ref[BND + rows :] = pltpu.roll(outflow[:BND], 127, 1)
        p_ref[:BND] = pltpu.roll(outflow[rows - BND :], 1, 1)
        arriving = cons_ref[5]
        for k in range(2 * BND + 1):
            arriving = arriving + w_ref[k] * p_ref[pl.ds(k, rows), :]
        waiting = queue + arriving
        entering = jnp.minimum(waiting, recv[0])
        queue = waiting - entering
        into = [entering] + inner
        leaving = inner + [outflow]
        new = [(rho[c] + into[c]) - leaving[c] for c in range(NC)]
        for c in range(NC):
            st_ref[c] = new[c]
        st_ref[NC] = queue
        occ = ((((new[0] + new[1]) + new[2]) + new[3]) + queue) / cap
        return acc + occ

    def interval(i, carry):
        acc = lax.fori_loop(0, ISTEPS, step, jnp.zeros((rows, 128), jnp.float32))
        occ_ref[i] = acc
        return carry

    lax.fori_loop(0, occ_ref.shape[0], interval, 0)


def simulate(st0, cons, count):
    rows = st0.shape[1]
    return pl.pallas_call(
        sim_kernel,
        out_shape=(
            jax.ShapeDtypeStruct((count, rows, 128), jnp.float32),
            jax.ShapeDtypeStruct(st0.shape, jnp.float32),
        ),
        scratch_shapes=[
            pltpu.VMEM((2 * BND + 1, rows, 128), jnp.float32),
            pltpu.VMEM((rows + 2 * BND, 128), jnp.float32),
        ],
    )(st0, cons)


def group_min(cost, group):
    reach = OD_MOST - 1
    count = cost.shape[0]
    padded_cost = jnp.pad(cost, reach, constant_values=1e30)
    padded_group = jnp.pad(group, reach, constant_values=-1)
    best = cost
    for shift in range(2 * reach + 1):
        near_cost = padded_cost[shift : shift + count]
        near_group = padded_group[shift : shift + count]
        best = jnp.minimum(best, jnp.where(near_group == group, near_cost, best))
    return best


def group_sum(values, group):
    reach = OD_MOST - 1
    count = values.shape[0]
    padded_values = jnp.pad(values, reach)
    padded_group = jnp.pad(group, reach, constant_values=-1)
    total = jnp.zeros_like(values)
    for shift in range(2 * reach + 1):
        near_values = padded_values[shift : shift + count]
        near_group = padded_group[shift : shift + count]
        total = total + jnp.where(near_group == group, near_values, 0.0)
    return total


def pick_rate(rate_num, group):
    count = rate_num.shape[0]
    table = rate_num.reshape(count // 128, 128).astype(jnp.float32)
    row_pick = ((group // 128)[:, None] == jnp.arange(count // 128)[None, :]).astype(jnp.float32)
    picked = jnp.dot(row_pick, table, precision=lax.Precision.HIGHEST, preferred_element_type=jnp.float32)
    lanes = jnp.arange(128, dtype=jnp.int32)
    return jnp.sum(jnp.where((group % 128)[:, None] == lanes[None, :], picked, 0.0), axis=1)


def swap_flows(cost, flow, group, rate):
    best = group_min(cost, group)
    moved = rate * flow * (cost - best) / cost
    pull = (best / cost) ** 4
    return flow - moved + group_sum(moved, group) * pull / group_sum(pull, group)


def select_depart(totals, depart_tile):
    levels = jnp.arange(totals.shape[1], dtype=jnp.int32)
    chosen = jnp.where(levels[None, :, None] == depart_tile[:, None, :], totals, 0.0)
    return jnp.sum(chosen, 1)


def body(
    fill,
    capacity,
    free_time,
    split_share,
    upstream_offset,
    path_flow,
    anchor,
    depart,
    od_pair,
    swap_rate,
    tile_index,
    incidence,
):
    span = fill.shape[1]
    paths = lax.all_gather(
        jnp.stack([path_flow, anchor.astype(jnp.float32)]), "route", axis=1, tiled=True
    )
    near = paths[1].astype(jnp.int32)
    own_tiles = jnp.arange(span // 128, dtype=jnp.int32) + lax.axis_index("route") * (span // 128)
    lanes = jnp.arange(128, dtype=jnp.int32)
    tile_pick = jnp.where((near // 128)[None, :] == own_tiles[:, None], paths[0][None, :], 0.0)
    lane_pick = ((near % 128)[:, None] == lanes[None, :]).astype(jnp.float32)
    entry = jnp.dot(
        tile_pick, lane_pick, precision=lax.Precision.HIGHEST, preferred_element_type=jnp.float32
    ).reshape(-1)
    width = halo_width(span)
    rows_in = jnp.concatenate(
        [fill, capacity[None], split_share, upstream_offset.astype(jnp.float32), entry[None]], 0
    )
    wide = padded(rows_in, width)
    wide_cap = wide[NC]
    st0 = jnp.concatenate([wide[:NC] * (4.0 * wide_cap), jnp.zeros_like(wide[:1])], 0)
    cons = wide[NC:]
    occ, state = simulate(to_cols(st0), to_cols(cons), NI)
    occ = from_cols(occ)[:, width : width + span]
    state = from_cols(state)[:NC, width : width + span]
    costs = free_time + occ / ISTEPS

    link_cost = costs.astype(jnp.bfloat16)
    tiles = link_cost.reshape(NI, span // 128, 128).transpose(1, 0, 2).reshape(span // 128, NI * 128)
    wanted_tiles = tile_index.reshape(-1)
    rate = pick_rate(swap_rate[0], od_pair[0]) / 16.0
    every_tile = lax.all_gather(tiles, "z", axis=0, tiled=True)
    piece = every_tile.shape[1] // 3
    every_tile = jnp.concatenate(
        [
            lax.all_gather(every_tile[:, c * piece : (c + 1) * piece], ("plane", "route"), axis=0, tiled=True)
            for c in range(3)
        ],
        1,
    )
    own = tiles.shape[0]
    planes = lax.axis_size(("plane", "route"))
    device = wanted_tiles // own
    wanted_tiles = (device % planes) * (lax.axis_size("z") * own) + (device // planes) * own + wanted_tiles % own
    fetched = every_tile[wanted_tiles]
    fetched = fetched.reshape(tile_index.shape[0], tile_index.shape[1], NI, 128)
    totals = jnp.einsum("ptil,ptlq->piq", fetched, incidence, preferred_element_type=jnp.float32)
    path_cost = select_depart(totals, depart.reshape(-1, 128)).reshape(-1) / 256.0
    new_flow = swap_flows(path_cost, path_flow, od_pair[0], rate)
    return (state, path_cost, new_flow)


def z_count(devices):
    try:
        return len({d.coords[2] for d in devices.flat})
    except (AttributeError, IndexError, TypeError):
        return 4


def solution(mesh):
    devices = mesh.devices
    count = z_count(devices)
    split = jax.sharding.Mesh(
        devices.reshape(count, devices.shape[0] // count, devices.shape[1]), LINE
    )
    return jax.shard_map(
        body,
        mesh=split,
        in_specs=(
            P(None, LINE),
            P(LINE),
            P(LINE),
            P(None, LINE),
            P(None, LINE),
            P(LINE),
            P(LINE),
            P(LINE),
            P(LINE, None),
            P(LINE, None),
            P(LINE, None),
            P(LINE, None, None, None),
        ),
        out_specs=(P(None, LINE), P(LINE), P(LINE)),
        check_vma=False,
    )
```

```python
import jax
import jax.numpy as jnp
from jax import lax
from jax.experimental import pallas as pl
from jax.experimental.pallas import tpu as pltpu
from jax.sharding import PartitionSpec as P

NC = 4
BND = 32
ISTEPS = 5
NI = 12
OD_MOST = 8
LINE = ("z", "plane", "route")


def halo_width(span):
    width = NI * ISTEPS * BND
    while (span + 2 * width) % 1024:
        width += 1
    return width


def padded(cells, width):
    count = lax.axis_size(LINE)
    head = cells[:, :width]
    tail = cells[:, cells.shape[1] - width :]
    return jnp.concatenate(
        [
            lax.ppermute(tail, LINE, [(i, (i + 1) % count) for i in range(count)]),
            cells,
            lax.ppermute(head, LINE, [((i + 1) % count, i) for i in range(count)]),
        ],
        axis=1,
    )


def to_cols(rows):
    extent = rows.shape[-1]
    lead = rows.shape[:-1]
    return jnp.swapaxes(rows.reshape(lead + (128, extent // 128)), -1, -2)


def from_cols(cols):
    lead = cols.shape[:-2]
    return jnp.swapaxes(cols, -1, -2).reshape(lead + (-1,))


def sim_kernel(st0_ref, cons_ref, occ_ref, st_ref, w_ref, p_ref):
    rows = st0_ref.shape[1]
    st_ref[...] = st0_ref[...]
    s0 = cons_ref[1]
    s1 = cons_ref[2]
    o0 = cons_ref[3]
    o1 = cons_ref[4]
    for k in range(2 * BND + 1):
        d = float(k - BND)
        w_ref[k] = jnp.where(o0 == d, s0, 0.0) + jnp.where(o1 == d, s1, 0.0)

    def step(j, acc):
        cap = cons_ref[0]
        jam = 4.0 * cap
        rho = [st_ref[c] for c in range(NC)]
        queue = st_ref[NC]
        send = [jnp.minimum(r, cap) for r in rho]
        recv = [jnp.minimum(cap, 0.5 * (jam - r)) for r in rho]
        inner = [jnp.minimum(send[c], recv[c + 1]) for c in range(NC - 1)]
        outflow = send[NC - 1]
        p_ref[BND : BND + rows] = outflow
        p_ref[BND + rows :] = pltpu.roll(outflow[:BND], 127, 1)
        p_ref[:BND] = pltpu.roll(outflow[rows - BND :], 1, 1)
        arriving = cons_ref[5]
        for k in range(2 * BND + 1):
            arriving = arriving + w_ref[k] * p_ref[pl.ds(k, rows), :]
        waiting = queue + arriving
        entering = jnp.minimum(waiting, recv[0])
        queue = waiting - entering
        into = [entering] + inner
        leaving = inner + [outflow]
        new = [(rho[c] + into[c]) - leaving[c] for c in range(NC)]
        for c in range(NC):
            st_ref[c] = new[c]
        st_ref[NC] = queue
        occ = ((((new[0] + new[1]) + new[2]) + new[3]) + queue) / cap
        return acc + occ

    def interval(i, carry):
        acc = lax.fori_loop(0, ISTEPS, step, jnp.zeros((rows, 128), jnp.float32))
        occ_ref[i] = acc
        return carry

    lax.fori_loop(0, occ_ref.shape[0], interval, 0)


def simulate(st0, cons, count):
    rows = st0.shape[1]
    return pl.pallas_call(
        sim_kernel,
        out_shape=(
            jax.ShapeDtypeStruct((count, rows, 128), jnp.float32),
            jax.ShapeDtypeStruct(st0.shape, jnp.float32),
        ),
        scratch_shapes=[
            pltpu.VMEM((2 * BND + 1, rows, 128), jnp.float32),
            pltpu.VMEM((rows + 2 * BND, 128), jnp.float32),
        ],
    )(st0, cons)


def group_min(cost, group):
    reach = OD_MOST - 1
    count = cost.shape[0]
    padded_cost = jnp.pad(cost, reach, constant_values=1e30)
    padded_group = jnp.pad(group, reach, constant_values=-1)
    best = cost
    for shift in range(2 * reach + 1):
        near_cost = padded_cost[shift : shift + count]
        near_group = padded_group[shift : shift + count]
        best = jnp.minimum(best, jnp.where(near_group == group, near_cost, best))
    return best


def group_sum(values, group):
    reach = OD_MOST - 1
    count = values.shape[0]
    padded_values = jnp.pad(values, reach)
    padded_group = jnp.pad(group, reach, constant_values=-1)
    total = jnp.zeros_like(values)
    for shift in range(2 * reach + 1):
        near_values = padded_values[shift : shift + count]
        near_group = padded_group[shift : shift + count]
        total = total + jnp.where(near_group == group, near_values, 0.0)
    return total


def pick_rate(rate_num, group):
    count = rate_num.shape[0]
    table = rate_num.reshape(count // 128, 128).astype(jnp.float32)
    row_pick = ((group // 128)[:, None] == jnp.arange(count // 128)[None, :]).astype(jnp.float32)
    picked = jnp.dot(row_pick, table, precision=lax.Precision.HIGHEST, preferred_element_type=jnp.float32)
    lanes = jnp.arange(128, dtype=jnp.int32)
    return jnp.sum(jnp.where((group % 128)[:, None] == lanes[None, :], picked, 0.0), axis=1)


def swap_flows(cost, flow, group, rate):
    best = group_min(cost, group)
    moved = rate * flow * (cost - best) / cost
    pull = (best / cost) ** 4
    return flow - moved + group_sum(moved, group) * pull / group_sum(pull, group)


def select_depart(totals, depart_tile):
    levels = jnp.arange(totals.shape[1], dtype=jnp.int32)
    chosen = jnp.where(levels[None, :, None] == depart_tile[:, None, :], totals, 0.0)
    return jnp.sum(chosen, 1)


def body(
    fill,
    capacity,
    free_time,
    split_share,
    upstream_offset,
    path_flow,
    anchor,
    depart,
    od_pair,
    swap_rate,
    tile_index,
    incidence,
):
    span = fill.shape[1]
    paths = lax.all_gather(
        jnp.stack([path_flow, anchor.astype(jnp.float32)]), "route", axis=1, tiled=True
    )
    near = paths[1].astype(jnp.int32)
    own_tiles = jnp.arange(span // 128, dtype=jnp.int32) + lax.axis_index("route") * (span // 128)
    lanes = jnp.arange(128, dtype=jnp.int32)
    tile_pick = jnp.where((near // 128)[None, :] == own_tiles[:, None], paths[0][None, :], 0.0)
    lane_pick = ((near % 128)[:, None] == lanes[None, :]).astype(jnp.float32)
    entry = jnp.dot(
        tile_pick, lane_pick, precision=lax.Precision.HIGHEST, preferred_element_type=jnp.float32
    ).reshape(-1)
    width = halo_width(span)
    rows_in = jnp.concatenate(
        [fill, capacity[None], split_share, upstream_offset.astype(jnp.float32), entry[None]], 0
    )
    wide = padded(rows_in, width)
    wide_cap = wide[NC]
    st0 = jnp.concatenate([wide[:NC] * (4.0 * wide_cap), jnp.zeros_like(wide[:1])], 0)
    cons = wide[NC:]
    occ, state = simulate(to_cols(st0), to_cols(cons), NI)
    occ = from_cols(occ)[:, width : width + span]
    state = from_cols(state)[:NC, width : width + span]
    costs = free_time + occ / ISTEPS

    link_cost = costs.astype(jnp.bfloat16)
    tiles = link_cost.reshape(NI, span // 128, 128).transpose(1, 0, 2).reshape(span // 128, NI * 128)
    wanted_tiles = tile_index.reshape(-1)
    rate = pick_rate(swap_rate[0], od_pair[0]) / 16.0
    zs = lax.axis_size("z")
    plane = ("plane", "route")
    blocks = [lax.all_gather(tiles, plane, axis=0, tiled=True)]
    moved = [lax.ppermute(tiles, "z", [((j + d) % zs, j) for j in range(zs)]) for d in range(1, zs)]
    blocks += [lax.all_gather(block, plane, axis=0, tiled=True) for block in moved]
    every_tile = jnp.concatenate(blocks, 0)
    own = tiles.shape[0]
    planes = lax.axis_size(plane)
    device = wanted_tiles // own
    shift = (device // planes - lax.axis_index("z")) % zs
    wanted_tiles = shift * (planes * own) + (device % planes) * own + wanted_tiles % own
    fetched = every_tile[wanted_tiles]
    fetched = fetched.reshape(tile_index.shape[0], tile_index.shape[1], NI, 128)
    totals = jnp.einsum("ptil,ptlq->piq", fetched, incidence, preferred_element_type=jnp.float32)
    path_cost = select_depart(totals, depart.reshape(-1, 128)).reshape(-1) / 256.0
    new_flow = swap_flows(path_cost, path_flow, od_pair[0], rate)
    return (state, path_cost, new_flow)


def z_count(devices):
    try:
        return len({d.coords[2] for d in devices.flat})
    except (AttributeError, IndexError, TypeError):
        return 4


def solution(mesh):
    devices = mesh.devices
    count = z_count(devices)
    split = jax.sharding.Mesh(
        devices.reshape(count, devices.shape[0] // count, devices.shape[1]), LINE
    )
    return jax.shard_map(
        body,
        mesh=split,
        in_specs=(
            P(None, LINE),
            P(LINE),
            P(LINE),
            P(None, LINE),
            P(None, LINE),
            P(LINE),
            P(LINE),
            P(LINE),
            P(LINE, None),
            P(LINE, None),
            P(LINE, None),
            P(LINE, None, None, None),
        ),
        out_specs=(P(None, LINE), P(LINE), P(LINE)),
        check_vma=False,
    )
```

```python
import jax
import jax.numpy as jnp
from jax import lax
from jax.experimental import pallas as pl
from jax.experimental.pallas import tpu as pltpu
from jax.sharding import PartitionSpec as P

NC = 4
BND = 32
ISTEPS = 5
NI = 12
OD_MOST = 8
LINE = ("z", "plane", "route")


def halo_width(span):
    width = NI * ISTEPS * BND
    while (span + 2 * width) % 1024:
        width += 1
    return width


def padded(cells, width):
    count = lax.axis_size(LINE)
    head = cells[:, :width]
    tail = cells[:, cells.shape[1] - width :]
    return jnp.concatenate(
        [
            lax.ppermute(tail, LINE, [(i, (i + 1) % count) for i in range(count)]),
            cells,
            lax.ppermute(head, LINE, [((i + 1) % count, i) for i in range(count)]),
        ],
        axis=1,
    )


def to_cols(rows):
    extent = rows.shape[-1]
    lead = rows.shape[:-1]
    return jnp.swapaxes(rows.reshape(lead + (128, extent // 128)), -1, -2)


def from_cols(cols):
    lead = cols.shape[:-2]
    return jnp.swapaxes(cols, -1, -2).reshape(lead + (-1,))


def sim_kernel(st0_ref, cons_ref, occ_ref, st_ref, w_ref, p_ref):
    rows = st0_ref.shape[1]
    st_ref[...] = st0_ref[...]
    s0 = cons_ref[1]
    s1 = cons_ref[2]
    o0 = cons_ref[3]
    o1 = cons_ref[4]
    for k in range(2 * BND + 1):
        d = float(k - BND)
        w_ref[k] = jnp.where(o0 == d, s0, 0.0) + jnp.where(o1 == d, s1, 0.0)

    def step(j, acc):
        cap = cons_ref[0]
        jam = 4.0 * cap
        rho = [st_ref[c] for c in range(NC)]
        queue = st_ref[NC]
        send = [jnp.minimum(r, cap) for r in rho]
        recv = [jnp.minimum(cap, 0.5 * (jam - r)) for r in rho]
        inner = [jnp.minimum(send[c], recv[c + 1]) for c in range(NC - 1)]
        outflow = send[NC - 1]
        p_ref[BND : BND + rows] = outflow
        p_ref[BND + rows :] = pltpu.roll(outflow[:BND], 127, 1)
        p_ref[:BND] = pltpu.roll(outflow[rows - BND :], 1, 1)
        arriving = cons_ref[5]
        for k in range(2 * BND + 1):
            arriving = arriving + w_ref[k] * p_ref[pl.ds(k, rows), :]
        waiting = queue + arriving
        entering = jnp.minimum(waiting, recv[0])
        queue = waiting - entering
        into = [entering] + inner
        leaving = inner + [outflow]
        new = [(rho[c] + into[c]) - leaving[c] for c in range(NC)]
        for c in range(NC):
            st_ref[c] = new[c]
        st_ref[NC] = queue
        occ = ((((new[0] + new[1]) + new[2]) + new[3]) + queue) / cap
        return acc + occ

    def interval(i, carry):
        acc = lax.fori_loop(0, ISTEPS, step, jnp.zeros((rows, 128), jnp.float32))
        occ_ref[i] = acc
        return carry

    lax.fori_loop(0, occ_ref.shape[0], interval, 0)


def simulate(st0, cons, count):
    rows = st0.shape[1]
    return pl.pallas_call(
        sim_kernel,
        out_shape=(
            jax.ShapeDtypeStruct((count, rows, 128), jnp.float32),
            jax.ShapeDtypeStruct(st0.shape, jnp.float32),
        ),
        scratch_shapes=[
            pltpu.VMEM((2 * BND + 1, rows, 128), jnp.float32),
            pltpu.VMEM((rows + 2 * BND, 128), jnp.float32),
        ],
    )(st0, cons)


def group_min(cost, group):
    reach = OD_MOST - 1
    count = cost.shape[0]
    padded_cost = jnp.pad(cost, reach, constant_values=1e30)
    padded_group = jnp.pad(group, reach, constant_values=-1)
    best = cost
    for shift in range(2 * reach + 1):
        near_cost = padded_cost[shift : shift + count]
        near_group = padded_group[shift : shift + count]
        best = jnp.minimum(best, jnp.where(near_group == group, near_cost, best))
    return best


def group_sum(values, group):
    reach = OD_MOST - 1
    count = values.shape[0]
    padded_values = jnp.pad(values, reach)
    padded_group = jnp.pad(group, reach, constant_values=-1)
    total = jnp.zeros_like(values)
    for shift in range(2 * reach + 1):
        near_values = padded_values[shift : shift + count]
        near_group = padded_group[shift : shift + count]
        total = total + jnp.where(near_group == group, near_values, 0.0)
    return total


def pick_rate(rate_num, group):
    count = rate_num.shape[0]
    table = rate_num.reshape(count // 128, 128).astype(jnp.float32)
    row_pick = ((group // 128)[:, None] == jnp.arange(count // 128)[None, :]).astype(jnp.float32)
    picked = jnp.dot(row_pick, table, precision=lax.Precision.HIGHEST, preferred_element_type=jnp.float32)
    lanes = jnp.arange(128, dtype=jnp.int32)
    return jnp.sum(jnp.where((group % 128)[:, None] == lanes[None, :], picked, 0.0), axis=1)


def swap_flows(cost, flow, group, rate):
    best = group_min(cost, group)
    moved = rate * flow * (cost - best) / cost
    pull = (best / cost) ** 4
    return flow - moved + group_sum(moved, group) * pull / group_sum(pull, group)


def select_depart(totals, depart_tile):
    levels = jnp.arange(totals.shape[1], dtype=jnp.int32)
    chosen = jnp.where(levels[None, :, None] == depart_tile[:, None, :], totals, 0.0)
    return jnp.sum(chosen, 1)


def body(
    fill,
    capacity,
    free_time,
    split_share,
    upstream_offset,
    path_flow,
    anchor,
    depart,
    od_pair,
    swap_rate,
    tile_index,
    incidence,
):
    span = fill.shape[1]
    paths = lax.all_gather(
        jnp.stack([path_flow, anchor.astype(jnp.float32)]), "route", axis=1, tiled=True
    )
    near = paths[1].astype(jnp.int32)
    own_tiles = jnp.arange(span // 128, dtype=jnp.int32) + lax.axis_index("route") * (span // 128)
    lanes = jnp.arange(128, dtype=jnp.int32)
    tile_pick = jnp.where((near // 128)[None, :] == own_tiles[:, None], paths[0][None, :], 0.0)
    lane_pick = ((near % 128)[:, None] == lanes[None, :]).astype(jnp.float32)
    entry = jnp.dot(
        tile_pick, lane_pick, precision=lax.Precision.HIGHEST, preferred_element_type=jnp.float32
    ).reshape(-1)
    width = halo_width(span)
    rows_in = jnp.concatenate(
        [fill, capacity[None], split_share, upstream_offset.astype(jnp.float32), entry[None]], 0
    )
    wide = padded(rows_in, width)
    wide_cap = wide[NC]
    st0 = jnp.concatenate([wide[:NC] * (4.0 * wide_cap), jnp.zeros_like(wide[:1])], 0)
    cons = wide[NC:]
    occ, state = simulate(to_cols(st0), to_cols(cons), NI)
    occ = from_cols(occ)[:, width : width + span]
    state = from_cols(state)[:NC, width : width + span]
    costs = free_time + occ / ISTEPS

    link_cost = costs.astype(jnp.bfloat16)
    tiles = link_cost.reshape(NI, span // 128, 128).transpose(1, 0, 2).reshape(span // 128, NI * 128)
    wanted_tiles = tile_index.reshape(-1)
    rate = pick_rate(swap_rate[0], od_pair[0]) / 16.0
    zs = lax.axis_size("z")
    plane = ("plane", "route")
    near = lax.all_gather(tiles, plane, axis=0, tiled=True)
    moved = jnp.concatenate(
        [lax.ppermute(tiles, "z", [((j + d) % zs, j) for j in range(zs)]) for d in range(1, zs)], 0
    )
    piece = moved.shape[1] // 2
    far = jnp.concatenate(
        [lax.all_gather(moved[:, c * piece : (c + 1) * piece], plane, axis=0, tiled=True) for c in range(2)],
        1,
    )
    every_tile = jnp.concatenate([near, far], 0)
    own = tiles.shape[0]
    planes = lax.axis_size(plane)
    device = wanted_tiles // own
    shift = (device // planes - lax.axis_index("z")) % zs
    inside = (device % planes) * own + wanted_tiles % own
    wanted_tiles = jnp.where(
        shift == 0,
        inside,
        planes * own + (device % planes) * ((zs - 1) * own) + (shift - 1) * own + wanted_tiles % own,
    )
    fetched = every_tile[wanted_tiles]
    fetched = fetched.reshape(tile_index.shape[0], tile_index.shape[1], NI, 128)
    totals = jnp.einsum("ptil,ptlq->piq", fetched, incidence, preferred_element_type=jnp.float32)
    path_cost = select_depart(totals, depart.reshape(-1, 128)).reshape(-1) / 256.0
    new_flow = swap_flows(path_cost, path_flow, od_pair[0], rate)
    return (state, path_cost, new_flow)


def z_count(devices):
    try:
        return len({d.coords[2] for d in devices.flat})
    except (AttributeError, IndexError, TypeError):
        return 4


def solution(mesh):
    devices = mesh.devices
    count = z_count(devices)
    split = jax.sharding.Mesh(
        devices.reshape(count, devices.shape[0] // count, devices.shape[1]), LINE
    )
    return jax.shard_map(
        body,
        mesh=split,
        in_specs=(
            P(None, LINE),
            P(LINE),
            P(LINE),
            P(None, LINE),
            P(None, LINE),
            P(LINE),
            P(LINE),
            P(LINE),
            P(LINE, None),
            P(LINE, None),
            P(LINE, None),
            P(LINE, None, None, None),
        ),
        out_specs=(P(None, LINE), P(LINE), P(LINE)),
        check_vma=False,
    )
```

```python
import jax
import jax.numpy as jnp
from jax import lax
from jax.experimental import pallas as pl
from jax.experimental.pallas import tpu as pltpu
from jax.sharding import PartitionSpec as P

NC = 4
BND = 32
ISTEPS = 5
NI = 12
OD_MOST = 8
LINE = ("z", "plane", "route")


def halo_width(span):
    width = NI * ISTEPS * BND
    while (span + 2 * width) % 1024:
        width += 1
    return width


def padded(cells, width):
    count = lax.axis_size(LINE)
    head = cells[:, :width]
    tail = cells[:, cells.shape[1] - width :]
    return jnp.concatenate(
        [
            lax.ppermute(tail, LINE, [(i, (i + 1) % count) for i in range(count)]),
            cells,
            lax.ppermute(head, LINE, [((i + 1) % count, i) for i in range(count)]),
        ],
        axis=1,
    )


def to_cols(rows):
    extent = rows.shape[-1]
    lead = rows.shape[:-1]
    return jnp.swapaxes(rows.reshape(lead + (128, extent // 128)), -1, -2)


def from_cols(cols):
    lead = cols.shape[:-2]
    return jnp.swapaxes(cols, -1, -2).reshape(lead + (-1,))


def sim_kernel(st0_ref, cons_ref, occ_ref, st_ref, w_ref, p_ref, half_ref, inv_ref):
    rows = st0_ref.shape[1]
    st_ref[...] = st0_ref[...]
    half_ref[...] = 2.0 * cons_ref[0]
    inv_ref[...] = 1.0 / cons_ref[0]
    s0 = cons_ref[1]
    s1 = cons_ref[2]
    o0 = cons_ref[3]
    o1 = cons_ref[4]
    for k in range(2 * BND + 1):
        d = float(k - BND)
        w_ref[k] = jnp.where(o0 == d, s0, 0.0) + jnp.where(o1 == d, s1, 0.0)

    def step(j, acc):
        cap = cons_ref[0]
        half_jam = half_ref[...]
        rho = [st_ref[c] for c in range(NC)]
        queue = st_ref[NC]
        send = [jnp.minimum(r, cap) for r in rho]
        recv = [jnp.minimum(cap, half_jam - 0.5 * r) for r in rho]
        inner = [jnp.minimum(send[c], recv[c + 1]) for c in range(NC - 1)]
        outflow = send[NC - 1]
        p_ref[BND : BND + rows] = outflow
        p_ref[BND + rows :] = pltpu.roll(outflow[:BND], 127, 1)
        p_ref[:BND] = pltpu.roll(outflow[rows - BND :], 1, 1)
        arriving = cons_ref[5]
        for k in range(2 * BND + 1):
            arriving = arriving + w_ref[k] * p_ref[pl.ds(k, rows), :]
        waiting = queue + arriving
        entering = jnp.minimum(waiting, recv[0])
        queue = waiting - entering
        into = [entering] + inner
        leaving = inner + [outflow]
        new = [(rho[c] + into[c]) - leaving[c] for c in range(NC)]
        for c in range(NC):
            st_ref[c] = new[c]
        st_ref[NC] = queue
        occ = ((((new[0] + new[1]) + new[2]) + new[3]) + queue) * inv_ref[...]
        return acc + occ

    def interval(i, carry):
        acc = lax.fori_loop(0, ISTEPS, step, jnp.zeros((rows, 128), jnp.float32))
        occ_ref[i] = acc
        return carry

    lax.fori_loop(0, occ_ref.shape[0], interval, 0)


def simulate(st0, cons, count):
    rows = st0.shape[1]
    return pl.pallas_call(
        sim_kernel,
        out_shape=(
            jax.ShapeDtypeStruct((count, rows, 128), jnp.float32),
            jax.ShapeDtypeStruct(st0.shape, jnp.float32),
        ),
        scratch_shapes=[
            pltpu.VMEM((2 * BND + 1, rows, 128), jnp.float32),
            pltpu.VMEM((rows + 2 * BND, 128), jnp.float32),
            pltpu.VMEM((rows, 128), jnp.float32),
            pltpu.VMEM((rows, 128), jnp.float32),
        ],
    )(st0, cons)


def group_min(cost, group):
    reach = OD_MOST - 1
    count = cost.shape[0]
    padded_cost = jnp.pad(cost, reach, constant_values=1e30)
    padded_group = jnp.pad(group, reach, constant_values=-1)
    best = cost
    for shift in range(2 * reach + 1):
        near_cost = padded_cost[shift : shift + count]
        near_group = padded_group[shift : shift + count]
        best = jnp.minimum(best, jnp.where(near_group == group, near_cost, best))
    return best


def group_sum(values, group):
    reach = OD_MOST - 1
    count = values.shape[0]
    padded_values = jnp.pad(values, reach)
    padded_group = jnp.pad(group, reach, constant_values=-1)
    total = jnp.zeros_like(values)
    for shift in range(2 * reach + 1):
        near_values = padded_values[shift : shift + count]
        near_group = padded_group[shift : shift + count]
        total = total + jnp.where(near_group == group, near_values, 0.0)
    return total


def pick_rate(rate_num, group):
    count = rate_num.shape[0]
    table = rate_num.reshape(count // 128, 128).astype(jnp.float32)
    row_pick = ((group // 128)[:, None] == jnp.arange(count // 128)[None, :]).astype(jnp.float32)
    picked = jnp.dot(row_pick, table, precision=lax.Precision.HIGHEST, preferred_element_type=jnp.float32)
    lanes = jnp.arange(128, dtype=jnp.int32)
    return jnp.sum(jnp.where((group % 128)[:, None] == lanes[None, :], picked, 0.0), axis=1)


def swap_flows(cost, flow, group, rate):
    best = group_min(cost, group)
    moved = rate * flow * (cost - best) / cost
    pull = (best / cost) ** 4
    return flow - moved + group_sum(moved, group) * pull / group_sum(pull, group)


def select_depart(totals, depart_tile):
    levels = jnp.arange(totals.shape[1], dtype=jnp.int32)
    chosen = jnp.where(levels[None, :, None] == depart_tile[:, None, :], totals, 0.0)
    return jnp.sum(chosen, 1)


def body(
    fill,
    capacity,
    free_time,
    split_share,
    upstream_offset,
    path_flow,
    anchor,
    depart,
    od_pair,
    swap_rate,
    tile_index,
    incidence,
):
    span = fill.shape[1]
    paths = lax.all_gather(
        jnp.stack([path_flow, anchor.astype(jnp.float32)]), "route", axis=1, tiled=True
    )
    near = paths[1].astype(jnp.int32)
    own_tiles = jnp.arange(span // 128, dtype=jnp.int32) + lax.axis_index("route") * (span // 128)
    lanes = jnp.arange(128, dtype=jnp.int32)
    tile_pick = jnp.where((near // 128)[None, :] == own_tiles[:, None], paths[0][None, :], 0.0)
    lane_pick = ((near % 128)[:, None] == lanes[None, :]).astype(jnp.float32)
    entry = jnp.dot(
        tile_pick, lane_pick, precision=lax.Precision.HIGHEST, preferred_element_type=jnp.float32
    ).reshape(-1)
    width = halo_width(span)
    rows_in = jnp.concatenate(
        [fill, capacity[None], split_share, upstream_offset.astype(jnp.float32), entry[None]], 0
    )
    wide = padded(rows_in, width)
    wide_cap = wide[NC]
    st0 = jnp.concatenate([wide[:NC] * (4.0 * wide_cap), jnp.zeros_like(wide[:1])], 0)
    cons = wide[NC:]
    occ, state = simulate(to_cols(st0), to_cols(cons), NI)
    occ = from_cols(occ)[:, width : width + span]
    state = from_cols(state)[:NC, width : width + span]
    costs = free_time + occ / ISTEPS

    link_cost = costs.astype(jnp.bfloat16)
    tiles = link_cost.reshape(NI, span // 128, 128).transpose(1, 0, 2).reshape(span // 128, NI * 128)
    wanted_tiles = tile_index.reshape(-1)
    rate = pick_rate(swap_rate[0], od_pair[0]) / 16.0
    zs = lax.axis_size("z")
    plane = ("plane", "route")
    near = lax.all_gather(tiles, plane, axis=0, tiled=True)
    moved = jnp.concatenate(
        [lax.ppermute(tiles, "z", [((j + d) % zs, j) for j in range(zs)]) for d in range(1, zs)], 0
    )
    piece = moved.shape[1] // 2
    far = jnp.concatenate(
        [lax.all_gather(moved[:, c * piece : (c + 1) * piece], plane, axis=0, tiled=True) for c in range(2)],
        1,
    )
    every_tile = jnp.concatenate([near, far], 0)
    own = tiles.shape[0]
    planes = lax.axis_size(plane)
    device = wanted_tiles // own
    shift = (device // planes - lax.axis_index("z")) % zs
    inside = (device % planes) * own + wanted_tiles % own
    wanted_tiles = jnp.where(
        shift == 0,
        inside,
        planes * own + (device % planes) * ((zs - 1) * own) + (shift - 1) * own + wanted_tiles % own,
    )
    fetched = every_tile[wanted_tiles]
    fetched = fetched.reshape(tile_index.shape[0], tile_index.shape[1], NI, 128)
    totals = jnp.einsum("ptil,ptlq->piq", fetched, incidence, preferred_element_type=jnp.float32)
    path_cost = select_depart(totals, depart.reshape(-1, 128)).reshape(-1) / 256.0
    new_flow = swap_flows(path_cost, path_flow, od_pair[0], rate)
    return (state, path_cost, new_flow)


def z_count(devices):
    try:
        return len({d.coords[2] for d in devices.flat})
    except (AttributeError, IndexError, TypeError):
        return 4


def solution(mesh):
    devices = mesh.devices
    count = z_count(devices)
    split = jax.sharding.Mesh(
        devices.reshape(count, devices.shape[0] // count, devices.shape[1]), LINE
    )
    return jax.shard_map(
        body,
        mesh=split,
        in_specs=(
            P(None, LINE),
            P(LINE),
            P(LINE),
            P(None, LINE),
            P(None, LINE),
            P(LINE),
            P(LINE),
            P(LINE),
            P(LINE, None),
            P(LINE, None),
            P(LINE, None),
            P(LINE, None, None, None),
        ),
        out_specs=(P(None, LINE), P(LINE), P(LINE)),
        check_vma=False,
    )
```
